256 devices in a mesh: row: 32 (over y, z), col: 8 (over x, core).
Axes of the slice: x: 4, y: 4, z: 8, core: 2. Of those that a mesh axis runs over, the one named last changes fastest.
Arguments:
- positions: float32 [2, 524288], P(None, ('row', 'col')), may hold values from 0 to 2048
- pin_offset: float32 [2, 256, 8192], P(None, ('row', 'col')), may hold values from -2 to 2
- net_weight: float32 [256, 2048], P(('row', 'col')), may hold values from 0.5 to 2
- pin_cell: int32 [256, 8192], P(('row', 'col')), may hold values from 0 to 2047
- pin_net: int32 [256, 8192], P(('row', 'col')), may hold values from 0 to 2047, never falling along the last dimension, each value on 1 to 24 neighbouring positions
- margin_bin: int32 [256, 256, 64], P(('row', 'col')), may hold values from 0 to 16383
- margin_area: float32 [256, 256, 64], P(('row', 'col')), may hold values from 0.1 to 1
- margin_cell: int32 [256, 256, 64], P(('row', 'col')), may hold values from 0 to 2047
Outputs:
- gradient: float32 [2, 524288], P(None, ('row', 'col'))
The draws below stay inside these ranges and needn't reach their ends.
Inputs may be any that keep to these rules, and one draw needn't show every extreme that they name: Within each block pin_net never falls and every net 0 .. 2047 has 1 to 24 pins.
All inputs are finite; a program needn't handle non-finite values.
Results may differ from the reference program's by a relative error of at most 0.0003.
Values sent between devices are 32-bit elements; how exact they have to be, the bound alone decides.
No kernel may reach another device: no remote copies, remote signals or barrier semaphores. Data moves between devices by JAX's collectives and lax.ppermute only.
A program may use at most 128 MiB of HBM per device.

```python
import math
import jax
import jax.numpy as jnp
import numpy as np
from jax import lax

NB = 2048
CELLS_DEV = 2048
NET_MOST = 24
NETS_DEV = 2048
PINS_DEV = 8192
CAP = 64
CELLS = 524288
N_ROW = 32
N_COL = 8
DEVICES = 256


def place_ends(entries, key, least, high):
    longest = entries.shape.index(max(entries.shape))
    spots = []
    for shift in (0, 1):
        where = [jax.random.randint(jax.random.fold_in(key, axis), (), 0, length) for axis, length in enumerate(entries.shape)]
        where[longest] = (where[longest] + shift) % entries.shape[longest]
        spots.append(tuple(where))
    return entries.at[spots[0]].set(least).at[spots[1]].set(high)


def shard_levels(key, dims, cuts, least, high):
    loudness = 1.0
    for dim, shards_of in cuts:
        draws = jax.random.uniform(jax.random.fold_in(jax.random.fold_in(key, 6), dim), (shards_of,), jnp.float32, least / len(cuts), high / len(cuts))
        loudness = loudness * jnp.repeat(jnp.exp(draws), dims[dim] // shards_of).reshape((-1,) + (1,) * (len(dims) - 1 - dim))
    return loudness


def length_profile(amount, total, bound, skew):
    loads = [(1 << 20) // math.isqrt(standing ** skew) + 1 for standing in range(2, amount + 1)]
    surplus, counts = total - bound - (amount - 1), [1] * (amount - 1)
    while surplus > 0:
        free = [i for i in range(amount - 1) if counts[i] < bound]
        mass, left = sum([loads[i] for i in free]), surplus
        for i in free:
            more = min(bound - counts[i], max(1, left * loads[i] // mass), surplus)
            counts[i] = counts[i] + more
            surplus = surplus - more
    return np.array([bound] + counts)


def ragged(rng, number_of, total, reach, lean):
    if number_of == 2:
        one = jax.random.randint(rng, (), max(1, total - reach), min(reach, total - 1) + 1)
        return jnp.stack([one, total - one])
    tallies = jnp.asarray(length_profile(number_of, total, reach, lean), jnp.int32)
    twos = (number_of - 1) // 2
    source_of, taker = tallies[1:1 + 2 * twos:2], tallies[2:2 + 2 * twos:2]
    margin = jnp.minimum(source_of - 1, reach - taker)
    shifted = jax.random.randint(jax.random.fold_in(rng, 1), (twos,), 0, 1 << 20) % (margin + 1)
    tallies = tallies.at[1:1 + 2 * twos:2].set(source_of - shifted).at[2:2 + 2 * twos:2].set(taker + shifted)
    return tallies[jax.random.permutation(jax.random.fold_in(rng, 2), number_of)]


def scatter_about(key, extent, width, bound, pieces=(), kind=jnp.bfloat16):
    result = width * jax.random.normal(key, extent, jnp.float32)
    if pieces:
        result = result * shard_levels(key, extent, pieces, -0.22, 0.18)
    return jnp.clip(result, -bound, bound).astype(kind)


def setup_inputs(seed: int = 0) -> dict:
    key_list = jax.random.split(jax.random.key(seed), 9)
    return {
        "positions": jnp.clip(2048.0 * jax.random.uniform(key_list[0], (2, CELLS), jnp.float32) ** shard_levels(key_list[0], (2, CELLS), ((1, 256),), -0.2, 0.2), 0.0, 2048.0),
        "pin_offset": scatter_about(key_list[1], (2, DEVICES, PINS_DEV), 0.5, 2.0, ((1, 256),), jnp.float32),
        "net_weight": jnp.clip(jnp.exp(math.log(2.0) - 1.3862944 * jax.random.uniform(key_list[2], (DEVICES, NETS_DEV), jnp.float32) ** shard_levels(key_list[2], (DEVICES, NETS_DEV), ((0, 256),), -0.2, 0.2)), 0.5, 2.0),
        "pin_cell": place_ends(jax.random.randint(key_list[3], (DEVICES, PINS_DEV), 0, CELLS_DEV), jax.random.fold_in(key_list[3], 1), 0, CELLS_DEV - 1).astype(jnp.int32),
        "pin_net": jax.vmap(lambda own: jnp.searchsorted(jnp.cumsum(ragged(own, NETS_DEV, PINS_DEV, NET_MOST, 1)), jnp.arange(PINS_DEV), side="right"))(jax.random.split(key_list[4], DEVICES)).reshape((DEVICES, PINS_DEV)).astype(jnp.int32),
        "margin_bin": place_ends(jax.random.randint(key_list[5], (DEVICES, DEVICES, CAP), 0, (NB // N_ROW) * (NB // N_COL)), jax.random.fold_in(key_list[5], 1), 0, ((NB // N_ROW) * (NB // N_COL)) - 1).astype(jnp.int32),
        "margin_area": jnp.clip(0.1 + 0.9 * jax.random.uniform(key_list[6], (DEVICES, DEVICES, CAP), jnp.float32) ** shard_levels(key_list[6], (DEVICES, DEVICES, CAP), ((0, 256),), -0.2, 0.2), 0.1, 1.0),
        "margin_cell": place_ends(jax.random.randint(key_list[7], (DEVICES, DEVICES, CAP), 0, CELLS_DEV), jax.random.fold_in(key_list[7], 1), 0, CELLS_DEV - 1).astype(jnp.int32),
    }


GAMMA_BINS = 8.0


def trig_tables(frequency, position, length):
    residue = (frequency * (2 * position + 1)) % (4 * length)
    angles = residue.astype(jnp.float32) * (jnp.pi / (2.0 * length))
    return jnp.cos(angles), jnp.sin(angles)


def spectral_scale(frequency):
    return jnp.where(frequency == 0, 1.0, 2.0).astype(jnp.float32) / NB


def field_weights(freq_u, freq_v):
    omega_u = freq_u.astype(jnp.float32) * (jnp.pi / NB)
    omega_v = freq_v.astype(jnp.float32) * (jnp.pi / NB)
    anchor = ((freq_u == 0) & (freq_v == 0)).astype(jnp.float32)
    denominator = omega_u * omega_u + omega_v * omega_v + anchor
    return omega_u / denominator, omega_v / denominator


def wirelength(cell_pos, offsets, weights, cell_ids, net_ids):
    num_nets = weights.shape[0]
    pin_pos = cell_pos[:, cell_ids] + offsets
    signed = jnp.concatenate([pin_pos, -pin_pos], axis=0)
    scores = signed / GAMMA_BINS

    def net_max(values):
        return jax.ops.segment_max(values, net_ids, num_segments=num_nets, indices_are_sorted=True)

    def net_sum(values):
        return jax.ops.segment_sum(values, net_ids, num_segments=num_nets, indices_are_sorted=True)

    maxima = jax.vmap(net_max)(scores)
    exp_terms = jnp.exp(scores - maxima[:, net_ids])
    totals = jax.vmap(net_sum)(exp_terms)
    moments = jax.vmap(net_sum)(signed * exp_terms)
    centres = moments / totals
    slopes = exp_terms / totals[:, net_ids] * (1.0 + (signed - centres[:, net_ids]) / GAMMA_BINS)
    pin_grad = (slopes[:2] - slopes[2:]) * weights[net_ids]
    return jnp.zeros((2, cell_pos.shape[1]), jnp.float32).at[:, cell_ids].add(pin_grad)


def highest_dot(left, right):
    return jnp.dot(left, right, precision=lax.Precision.HIGHEST, preferred_element_type=jnp.float32)


def reference(positions, pin_offset, net_weight, pin_cell, pin_net, margin_bin, margin_area, margin_cell):
    blocks = DEVICES
    wire_grad = jax.vmap(wirelength, in_axes=(1, 1, 0, 0, 0), out_axes=1)(
        positions.reshape(2, blocks, CELLS_DEV), pin_offset, net_weight, pin_cell, pin_net)
    tile_rows = NB // N_ROW
    tile_cols = NB // N_COL

    def deposit(bin_ids, areas):
        return jnp.zeros((tile_rows * tile_cols,), jnp.float32).at[bin_ids.reshape(-1)].add(areas.reshape(-1))

    tiles = jax.vmap(deposit)(margin_bin, margin_area)
    density = tiles.reshape(N_ROW, N_COL, tile_rows, tile_cols).transpose(0, 2, 1, 3).reshape(NB, NB)
    indices = jnp.arange(NB, dtype=jnp.int32)
    cosine_table, sine_table = trig_tables(indices[:, None], indices[None, :], NB)
    scaling = spectral_scale(indices)
    coeffs = highest_dot(highest_dot(cosine_table, density), cosine_table.T) * scaling[:, None] * scaling[None, :]
    weight_x, weight_y = field_weights(indices[:, None], indices[None, :])
    field_x = highest_dot(highest_dot(sine_table.T, coeffs * weight_x), cosine_table)
    field_y = highest_dot(highest_dot(cosine_table.T, coeffs * weight_y), sine_table)

    def to_tiles(field):
        return field.reshape(N_ROW, tile_rows, N_COL, tile_cols).transpose(0, 2, 1, 3).reshape(blocks, tile_rows * tile_cols)

    def pick(flat, bin_ids):
        return flat[bin_ids]

    push_x = -margin_area * jax.vmap(pick)(to_tiles(field_x), margin_bin)
    push_y = -margin_area * jax.vmap(pick)(to_tiles(field_y), margin_bin)

    def collect(cell_ids, values_x, values_y):
        empty = jnp.zeros((2, CELLS_DEV), jnp.float32)
        return empty.at[0, cell_ids].add(values_x).at[1, cell_ids].add(values_y)

    density_grad = jax.vmap(collect)(margin_cell, push_x.transpose(1, 0, 2), push_y.transpose(1, 0, 2))
    total = wire_grad + density_grad.transpose(1, 0, 2)
    return total.reshape(2, CELLS)
```

```python
import jax
import jax.numpy as jnp
from jax import lax
from jax.sharding import PartitionSpec as P

NB = 2048


GAMMA_BINS = 8.0
HIGH = lax.Precision.HIGH
HIGHEST = lax.Precision.HIGHEST
STEPS = (1, 2, 4, 8, 16)


def trig_tables(frequency, position, length):
    residue = frequency * (2 * position + 1) % (4 * length)
    angles = residue.astype(jnp.float32) * (jnp.pi / (2.0 * length))
    return (jnp.cos(angles), jnp.sin(angles))


def full_tables(length):
    odd = 2 * lax.optimization_barrier(jnp.arange(length, dtype=jnp.int32)) + 1
    upper = (jnp.arange(length // 32, dtype=jnp.int32) * 32)[:, None] * odd[None, :] % (4 * length)
    lower = jnp.arange(32, dtype=jnp.int32)[:, None] * odd[None, :] % (4 * length)
    step = jnp.pi / (2.0 * length)
    cos_a, sin_a = jnp.cos(upper.astype(jnp.float32) * step), jnp.sin(upper.astype(jnp.float32) * step)
    cos_b, sin_b = jnp.cos(lower.astype(jnp.float32) * step), jnp.sin(lower.astype(jnp.float32) * step)
    cosine = cos_a[:, None, :] * cos_b[None, :, :] - sin_a[:, None, :] * sin_b[None, :, :]
    sine = sin_a[:, None, :] * cos_b[None, :, :] + cos_a[:, None, :] * sin_b[None, :, :]
    return cosine.reshape(length, length), sine.reshape(length, length)


def spectral_scale(frequency):
    return jnp.where(frequency == 0, 1.0, 2.0).astype(jnp.float32) / NB


def field_weights(freq_u, freq_v):
    omega_u = freq_u.astype(jnp.float32) * (jnp.pi / NB)
    omega_v = freq_v.astype(jnp.float32) * (jnp.pi / NB)
    anchor = ((freq_u == 0) & (freq_v == 0)).astype(jnp.float32)
    denominator = omega_u * omega_u + omega_v * omega_v + anchor
    return (omega_u / denominator, omega_v / denominator)


def dot(left, right, precision):
    return jnp.dot(left, right, precision=precision, preferred_element_type=jnp.float32)


def dot_t(left, right, precision):
    return lax.dot_general(
        left, right, (((0,), (0,)), ((), ())), precision=precision,
        preferred_element_type=jnp.float32,
    )


def one_hot(ids, count):
    return (ids[:, None] == jnp.arange(count, dtype=ids.dtype)[None, :]).astype(jnp.float32)


def gather_rows(values, ids, precision):
    channels, size = values.shape
    table = values.reshape(channels, size // 128, 128).transpose(1, 0, 2).reshape(size // 128, channels * 128)
    picked = dot(one_hot(ids // 128, size // 128), table, precision).reshape(ids.shape[0], channels, 128)
    lane = (ids % 128)[:, None, None] == jnp.arange(128, dtype=ids.dtype)[None, None, :]
    return jnp.sum(jnp.where(lane, picked, 0.0), axis=-1)


def scatter_rows(values, ids, size, precision):
    count, channels = values.shape
    lane = one_hot(ids % 128, 128)
    spread = (values[:, :, None] * lane[:, None, :]).reshape(count, channels * 128)
    summed = dot_t(one_hot(ids // 128, size // 128), spread, precision)
    return summed.reshape(size // 128, channels, 128).transpose(1, 0, 2).reshape(channels, size)


def shift_prev(x, s, fill):
    pad = jnp.full(x.shape[:-1] + (s,), fill, x.dtype)
    return jnp.concatenate([pad, x[..., :-s]], axis=-1)


def shift_next(x, s, fill):
    pad = jnp.full(x.shape[:-1] + (s,), fill, x.dtype)
    return jnp.concatenate([x[..., s:], pad], axis=-1)


def wirelength(cell_pos, offsets, weights, cell_ids, net_ids):
    pin_pos = gather_rows(cell_pos, cell_ids, HIGHEST).T + offsets
    signed = jnp.concatenate([pin_pos, -pin_pos], axis=0)
    scores = signed / GAMMA_BINS
    prev_same = [shift_prev(net_ids, s, -1) == net_ids for s in STEPS]
    next_same = [shift_next(net_ids, s, -1) == net_ids for s in STEPS]
    maxima = scores
    for s, same in zip(STEPS, prev_same):
        maxima = jnp.where(same, jnp.maximum(maxima, shift_prev(maxima, s, 0.0)), maxima)
    for s, same in zip(STEPS, next_same):
        maxima = jnp.where(same, jnp.maximum(maxima, shift_next(maxima, s, 0.0)), maxima)
    exp_terms = jnp.exp(scores - maxima)
    sums = jnp.concatenate([exp_terms, signed * exp_terms], axis=0)
    for s, same in zip(STEPS, prev_same):
        sums = sums + jnp.where(same, shift_prev(sums, s, 0.0), 0.0)
    for s, same in zip(STEPS, next_same):
        sums = jnp.where(same, shift_next(sums, s, 0.0), sums)
    totals = sums[:4]
    centres = sums[4:] / totals
    slopes = exp_terms / totals * (1.0 + (signed - centres) / GAMMA_BINS)
    pin_weight = gather_rows(weights[None, :], net_ids, HIGHEST)[:, 0]
    return (slopes[:2] - slopes[2:]) * pin_weight


def local(
    positions, pin_offset, net_weight, pin_cell, pin_net, margin_bin, margin_area, margin_cell
):
    pin_grad = wirelength(positions, pin_offset[:, 0, :], net_weight[0], pin_cell[0], pin_net[0])
    n_rows = lax.axis_size("row")
    n_cols = lax.axis_size("col")
    tile_rows = NB // n_rows
    tile_cols = NB // n_cols
    row_index = lax.axis_index("row")
    col_index = lax.axis_index("col")
    bin_ids = margin_bin[0].reshape(-1)
    areas = margin_area[0].reshape(-1)
    tile_size = tile_rows * tile_cols
    density = scatter_rows(areas[:, None], bin_ids, tile_size, HIGH).reshape(tile_rows, tile_cols)
    cols_mine = col_index * tile_cols + jnp.arange(tile_cols, dtype=jnp.int32)
    part_in = lax.all_gather(density, "col", axis=1, tiled=True)
    places = jnp.arange(part_in.shape[1], dtype=jnp.int32)
    cosine_table, sine_table = trig_tables(cols_mine[None, :], places[:, None], NB)
    spectral = dot(part_in, cosine_table, HIGH)
    spectral = spectral * spectral_scale(cols_mine)[None, :]
    strip = lax.all_to_all(spectral, "row", split_axis=1, concat_axis=0, tiled=True)
    width = tile_cols // n_rows
    v_mine = col_index * tile_cols + row_index * width + jnp.arange(width, dtype=jnp.int32)
    frequency = jnp.arange(NB, dtype=jnp.int32)
    cosine_full, sine_full = full_tables(NB)
    coeffs = dot(cosine_full, strip, HIGH) * spectral_scale(frequency)[:, None]
    weight_x, weight_y = field_weights(frequency[:, None], v_mine[None, :])
    grad_x = dot_t(sine_full, coeffs * weight_x, HIGH)
    grad_y = dot_t(cosine_full, coeffs * weight_y, HIGH)
    stacked = jnp.stack([grad_x, grad_y], axis=1)
    back = lax.all_to_all(stacked, "row", split_axis=0, concat_axis=2, tiled=True)
    pieces = lax.all_gather(back, "col", axis=2, tiled=True)
    cosine_table, sine_table = trig_tables(frequency[:, None], cols_mine[None, :], NB)
    field_x = dot(pieces[:, 0, :], cosine_table, HIGH)
    field_y = dot(pieces[:, 1, :], sine_table, HIGH)
    fields = jnp.stack([field_x.reshape(-1), field_y.reshape(-1)], axis=0)
    push = -areas[:, None] * gather_rows(fields, bin_ids, HIGH)
    slot_count = margin_bin.shape[2]
    outgoing = push.reshape(n_rows, n_cols, 2 * slot_count)
    incoming = lax.all_to_all(
        lax.all_to_all(outgoing, "row", split_axis=0, concat_axis=0, tiled=True),
        "col",
        split_axis=1,
        concat_axis=1,
        tiled=True,
    )
    owners = margin_cell[0].reshape(-1)
    ids = jnp.concatenate([pin_cell[0], owners])
    values = jnp.concatenate([pin_grad.T, incoming.reshape(-1, 2)], axis=0)
    return scatter_rows(values, ids, positions.shape[1], HIGH)


def solution(mesh):
    placed = (
        P(None, ("row", "col")),
        P(None, ("row", "col"), None),
        P(("row", "col"), None),
        P(("row", "col"), None),
        P(("row", "col"), None),
        P(("row", "col"), None, None),
        P(("row", "col"), None, None),
        P(("row", "col"), None, None),
    )
    return jax.shard_map(
        local, mesh=mesh, in_specs=placed, out_specs=P(None, ("row", "col")), check_vma=False
    )
```

```python
import jax
import jax.numpy as jnp
from jax import lax
from jax.sharding import PartitionSpec as P

NB = 2048


GAMMA_BINS = 8.0
HIGH = lax.Precision.HIGH
HIGHEST = lax.Precision.HIGHEST
STEPS = (1, 2, 4, 8, 16)


def trig_tables(frequency, position, length):
    residue = frequency * (2 * position + 1) % (4 * length)
    angles = residue.astype(jnp.float32) * (jnp.pi / (2.0 * length))
    return (jnp.cos(angles), jnp.sin(angles))


def full_tables(length):
    odd = 2 * lax.optimization_barrier(jnp.arange(length, dtype=jnp.int32)) + 1
    upper = (jnp.arange(length // 32, dtype=jnp.int32) * 32)[:, None] * odd[None, :] % (4 * length)
    lower = jnp.arange(32, dtype=jnp.int32)[:, None] * odd[None, :] % (4 * length)
    step = jnp.pi / (2.0 * length)
    cos_a, sin_a = jnp.cos(upper.astype(jnp.float32) * step), jnp.sin(upper.astype(jnp.float32) * step)
    cos_b, sin_b = jnp.cos(lower.astype(jnp.float32) * step), jnp.sin(lower.astype(jnp.float32) * step)
    cosine = cos_a[:, None, :] * cos_b[None, :, :] - sin_a[:, None, :] * sin_b[None, :, :]
    sine = sin_a[:, None, :] * cos_b[None, :, :] + cos_a[:, None, :] * sin_b[None, :, :]
    return cosine.reshape(length, length), sine.reshape(length, length)


def spectral_scale(frequency):
    return jnp.where(frequency == 0, 1.0, 2.0).astype(jnp.float32) / NB


def field_weights(freq_u, freq_v):
    omega_u = freq_u.astype(jnp.float32) * (jnp.pi / NB)
    omega_v = freq_v.astype(jnp.float32) * (jnp.pi / NB)
    anchor = ((freq_u == 0) & (freq_v == 0)).astype(jnp.float32)
    denominator = omega_u * omega_u + omega_v * omega_v + anchor
    return (omega_u / denominator, omega_v / denominator)


def dot(left, right, precision):
    return jnp.dot(left, right, precision=precision, preferred_element_type=jnp.float32)


def dot_t(left, right, precision):
    return lax.dot_general(
        left, right, (((0,), (0,)), ((), ())), precision=precision,
        preferred_element_type=jnp.float32,
    )


def one_hot(ids, count):
    return (ids[:, None] == jnp.arange(count, dtype=ids.dtype)[None, :]).astype(jnp.float32)


def gather_rows(values, ids, precision):
    channels, size = values.shape
    table = values.reshape(channels, size // 128, 128).transpose(1, 0, 2).reshape(size // 128, channels * 128)
    picked = lax.dot_general(
        table, one_hot(ids // 128, size // 128), (((0,), (1,)), ((), ())), precision=precision,
        preferred_element_type=jnp.float32,
    ).reshape(channels, 128, ids.shape[0])
    lane = jnp.arange(128, dtype=ids.dtype)[:, None] == (ids % 128)[None, :]
    return jnp.sum(jnp.where(lane[None], picked, 0.0), axis=1)


def scatter_rows(values, ids, size, precision):
    channels, count = values.shape
    lane = (jnp.arange(128, dtype=ids.dtype)[:, None] == (ids % 128)[None, :]).astype(jnp.float32)
    spread = (values[:, None, :] * lane[None, :, :]).reshape(channels * 128, count)
    summed = dot(spread, one_hot(ids // 128, size // 128), precision)
    return summed.reshape(channels, 128, size // 128).transpose(0, 2, 1).reshape(channels, size)


def shift_prev(x, s, fill):
    pad = jnp.full(x.shape[:-1] + (s,), fill, x.dtype)
    return jnp.concatenate([pad, x[..., :-s]], axis=-1)


def shift_next(x, s, fill):
    pad = jnp.full(x.shape[:-1] + (s,), fill, x.dtype)
    return jnp.concatenate([x[..., s:], pad], axis=-1)


def wirelength(cell_pos, offsets, weights, cell_ids, net_ids):
    pin_pos = gather_rows(cell_pos, cell_ids, HIGHEST) + offsets
    signed = jnp.concatenate([pin_pos, -pin_pos], axis=0)
    scores = signed / GAMMA_BINS
    prev_same = [shift_prev(net_ids, s, -1) == net_ids for s in STEPS]
    next_same = [shift_next(net_ids, s, -1) == net_ids for s in STEPS]
    maxima = scores
    for s, same in zip(STEPS, prev_same):
        maxima = jnp.where(same, jnp.maximum(maxima, shift_prev(maxima, s, 0.0)), maxima)
    for s, same in zip(STEPS, next_same):
        maxima = jnp.where(same, jnp.maximum(maxima, shift_next(maxima, s, 0.0)), maxima)
    exp_terms = jnp.exp(scores - maxima)
    sums = jnp.concatenate([exp_terms, signed * exp_terms], axis=0)
    for s, same in zip(STEPS, prev_same):
        sums = sums + jnp.where(same, shift_prev(sums, s, 0.0), 0.0)
    for s, same in zip(STEPS, next_same):
        sums = jnp.where(same, shift_next(sums, s, 0.0), sums)
    totals = sums[:4]
    centres = sums[4:] / totals
    slopes = exp_terms / totals * (1.0 + (signed - centres) / GAMMA_BINS)
    pin_weight = gather_rows(weights[None, :], net_ids, HIGHEST)[0]
    return (slopes[:2] - slopes[2:]) * pin_weight


def local(
    positions, pin_offset, net_weight, pin_cell, pin_net, margin_bin, margin_area, margin_cell
):
    pin_grad = wirelength(positions, pin_offset[:, 0, :], net_weight[0], pin_cell[0], pin_net[0])
    n_rows = lax.axis_size("row")
    n_cols = lax.axis_size("col")
    tile_rows = NB // n_rows
    tile_cols = NB // n_cols
    row_index = lax.axis_index("row")
    col_index = lax.axis_index("col")
    bin_ids = margin_bin[0].reshape(-1)
    areas = margin_area[0].reshape(-1)
    tile_size = tile_rows * tile_cols
    density = scatter_rows(areas[None, :], bin_ids, tile_size, HIGH).reshape(tile_rows, tile_cols)
    cosine_full, sine_full = full_tables(NB)
    start = col_index * tile_cols
    part_in = lax.all_gather(density, "col", axis=1, tiled=True)
    cosine_rows = lax.dynamic_slice_in_dim(cosine_full, start, tile_cols, axis=0)
    spectral = lax.dot_general(
        part_in, cosine_rows, (((1,), (1,)), ((), ())), precision=HIGH,
        preferred_element_type=jnp.float32,
    )
    cols_mine = start + jnp.arange(tile_cols, dtype=jnp.int32)
    spectral = spectral * spectral_scale(cols_mine)[None, :]
    strip = lax.all_to_all(spectral, "row", split_axis=1, concat_axis=0, tiled=True)
    width = tile_cols // n_rows
    v_mine = start + row_index * width + jnp.arange(width, dtype=jnp.int32)
    frequency = jnp.arange(NB, dtype=jnp.int32)
    coeffs = dot(cosine_full, strip, HIGH) * spectral_scale(frequency)[:, None]
    weight_x, weight_y = field_weights(frequency[:, None], v_mine[None, :])
    grad_x = dot_t(sine_full, coeffs * weight_x, HIGH)
    grad_y = dot_t(cosine_full, coeffs * weight_y, HIGH)
    stacked = jnp.stack([grad_x, grad_y], axis=1)
    back = lax.all_to_all(stacked, "row", split_axis=0, concat_axis=2, tiled=True)
    pieces = lax.all_gather(back, "col", axis=2, tiled=True)
    cosine_cols = lax.dynamic_slice_in_dim(cosine_full, start, tile_cols, axis=1)
    sine_cols = lax.dynamic_slice_in_dim(sine_full, start, tile_cols, axis=1)
    field_x = dot(pieces[:, 0, :], cosine_cols, HIGH)
    field_y = dot(pieces[:, 1, :], sine_cols, HIGH)
    fields = jnp.stack([field_x.reshape(-1), field_y.reshape(-1)], axis=0)
    push = -areas[None, :] * gather_rows(fields, bin_ids, HIGH)
    slot_count = margin_bin.shape[2]
    blocks = n_rows * n_cols
    outgoing = push.reshape(2, blocks, slot_count).transpose(1, 0, 2).reshape(blocks, 2 * slot_count)
    incoming = lax.all_to_all(outgoing, ("row", "col"), split_axis=0, concat_axis=0, tiled=True)
    incoming = incoming.reshape(blocks, 2, slot_count).transpose(1, 0, 2).reshape(2, blocks * slot_count)
    owners = margin_cell[0].reshape(-1)
    ids = jnp.concatenate([pin_cell[0], owners])
    values = jnp.concatenate([pin_grad, incoming], axis=1)
    return scatter_rows(values, ids, positions.shape[1], HIGH)


def solution(mesh):
    placed = (
        P(None, ("row", "col")),
        P(None, ("row", "col"), None),
        P(("row", "col"), None),
        P(("row", "col"), None),
        P(("row", "col"), None),
        P(("row", "col"), None, None),
        P(("row", "col"), None, None),
        P(("row", "col"), None, None),
    )
    return jax.shard_map(
        local, mesh=mesh, in_specs=placed, out_specs=P(None, ("row", "col")), check_vma=False
    )
```

```python
import jax
import jax.numpy as jnp
from jax import lax
from jax.sharding import PartitionSpec as P

NB = 2048


GAMMA_BINS = 8.0
HIGH = lax.Precision.HIGH
HIGHEST = lax.Precision.HIGHEST
STEPS = (1, 2, 4, 8, 16)


def trig_tables(frequency, position, length):
    residue = frequency * (2 * position + 1) % (4 * length)
    angles = residue.astype(jnp.float32) * (jnp.pi / (2.0 * length))
    return (jnp.cos(angles), jnp.sin(angles))


def full_tables(length):
    odd = 2 * lax.optimization_barrier(jnp.arange(length, dtype=jnp.int32)) + 1
    upper = (jnp.arange(length // 32, dtype=jnp.int32) * 32)[:, None] * odd[None, :] % (4 * length)
    lower = jnp.arange(32, dtype=jnp.int32)[:, None] * odd[None, :] % (4 * length)
    step = jnp.pi / (2.0 * length)
    cos_a, sin_a = jnp.cos(upper.astype(jnp.float32) * step), jnp.sin(upper.astype(jnp.float32) * step)
    cos_b, sin_b = jnp.cos(lower.astype(jnp.float32) * step), jnp.sin(lower.astype(jnp.float32) * step)
    cosine = cos_a[:, None, :] * cos_b[None, :, :] - sin_a[:, None, :] * sin_b[None, :, :]
    sine = sin_a[:, None, :] * cos_b[None, :, :] + cos_a[:, None, :] * sin_b[None, :, :]
    return cosine.reshape(length, length), sine.reshape(length, length)


def spectral_scale(frequency):
    return jnp.where(frequency == 0, 1.0, 2.0).astype(jnp.float32) / NB


def field_weights(freq_u, freq_v):
    omega_u = freq_u.astype(jnp.float32) * (jnp.pi / NB)
    omega_v = freq_v.astype(jnp.float32) * (jnp.pi / NB)
    anchor = ((freq_u == 0) & (freq_v == 0)).astype(jnp.float32)
    denominator = omega_u * omega_u + omega_v * omega_v + anchor
    return (omega_u / denominator, omega_v / denominator)


def dot(left, right, precision):
    return jnp.dot(left, right, precision=precision, preferred_element_type=jnp.float32)


def dot_t(left, right, precision):
    return lax.dot_general(
        left, right, (((0,), (0,)), ((), ())), precision=precision,
        preferred_element_type=jnp.float32,
    )


def one_hot(ids, count):
    return (ids[:, None] == jnp.arange(count, dtype=ids.dtype)[None, :]).astype(jnp.float32)


def gather_rows(values, ids, precision):
    channels, size = values.shape
    table = values.reshape(channels, size // 128, 128).transpose(1, 0, 2).reshape(size // 128, channels * 128)
    picked = lax.dot_general(
        table, one_hot(ids // 128, size // 128), (((0,), (1,)), ((), ())), precision=precision,
        preferred_element_type=jnp.float32,
    ).reshape(channels, 128, ids.shape[0])
    lane = jnp.arange(128, dtype=ids.dtype)[:, None] == (ids % 128)[None, :]
    return jnp.sum(jnp.where(lane[None], picked, 0.0), axis=1)


def scatter_rows(values, ids, size, precision):
    channels, count = values.shape
    lane = (jnp.arange(128, dtype=ids.dtype)[:, None] == (ids % 128)[None, :]).astype(jnp.float32)
    spread = (values[:, None, :] * lane[None, :, :]).reshape(channels * 128, count)
    summed = dot(spread, one_hot(ids // 128, size // 128), precision)
    return summed.reshape(channels, 128, size // 128).transpose(0, 2, 1).reshape(channels, size)


def shift_prev(x, s, fill):
    pad = jnp.full(x.shape[:-1] + (s,), fill, x.dtype)
    return jnp.concatenate([pad, x[..., :-s]], axis=-1)


def shift_next(x, s, fill):
    pad = jnp.full(x.shape[:-1] + (s,), fill, x.dtype)
    return jnp.concatenate([x[..., s:], pad], axis=-1)


def wirelength(cell_pos, offsets, weights, cell_ids, net_ids):
    pin_pos = gather_rows(cell_pos, cell_ids, HIGHEST) + offsets
    signed = jnp.concatenate([pin_pos, -pin_pos], axis=0)
    scores = signed / GAMMA_BINS
    prev_same = [shift_prev(net_ids, s, -1) == net_ids for s in STEPS]
    next_same = [shift_next(net_ids, s, -1) == net_ids for s in STEPS]
    maxima = scores
    for s, same in zip(STEPS, prev_same):
        maxima = jnp.where(same, jnp.maximum(maxima, shift_prev(maxima, s, 0.0)), maxima)
    for s, same in zip(STEPS, next_same):
        maxima = jnp.where(same, jnp.maximum(maxima, shift_next(maxima, s, 0.0)), maxima)
    exp_terms = jnp.exp(scores - maxima)
    sums = jnp.concatenate([exp_terms, signed * exp_terms], axis=0)
    for s, same in zip(STEPS, prev_same):
        sums = sums + jnp.where(same, shift_prev(sums, s, 0.0), 0.0)
    for s, same in zip(STEPS, next_same):
        sums = jnp.where(same, shift_next(sums, s, 0.0), sums)
    totals = sums[:4]
    centres = sums[4:] / totals
    slopes = exp_terms / totals * (1.0 + (signed - centres) / GAMMA_BINS)
    pin_weight = gather_rows(weights[None, :], net_ids, HIGHEST)[0]
    return (slopes[:2] - slopes[2:]) * pin_weight


def local(
    positions, pin_offset, net_weight, pin_cell, pin_net, margin_bin, margin_area, margin_cell
):
    pin_grad = wirelength(positions, pin_offset[:, 0, :], net_weight[0], pin_cell[0], pin_net[0])
    n_rows = lax.axis_size("row")
    n_cols = lax.axis_size("col")
    tile_rows = NB // n_rows
    tile_cols = NB // n_cols
    row_index = lax.axis_index("row")
    col_index = lax.axis_index("col")
    bin_ids = margin_bin[0].reshape(-1)
    areas = margin_area[0].reshape(-1)
    tile_size = tile_rows * tile_cols
    density = scatter_rows(areas[None, :], bin_ids, tile_size, HIGH).reshape(tile_rows, tile_cols)
    cosine_full, sine_full = full_tables(NB)
    start = col_index * tile_cols
    part_in = lax.all_gather(density, "col", axis=1, tiled=True)
    cosine_rows = lax.dynamic_slice_in_dim(cosine_full, start, tile_cols, axis=0)
    cols_mine = start + jnp.arange(tile_cols, dtype=jnp.int32)
    spectral = lax.dot_general(
        cosine_rows, part_in, (((1,), (1,)), ((), ())), precision=HIGH,
        preferred_element_type=jnp.float32,
    ) * spectral_scale(cols_mine)[:, None]
    strip = lax.all_to_all(spectral, "row", split_axis=0, concat_axis=1, tiled=True)
    width = tile_cols // n_rows
    v_mine = start + row_index * width + jnp.arange(width, dtype=jnp.int32)
    frequency = jnp.arange(NB, dtype=jnp.int32)
    coeffs = lax.dot_general(
        strip, cosine_full, (((1,), (1,)), ((), ())), precision=HIGH,
        preferred_element_type=jnp.float32,
    ) * spectral_scale(frequency)[None, :]
    weight_x, weight_y = field_weights(frequency[None, :], v_mine[:, None])
    grad_x = dot(coeffs * weight_x, sine_full, HIGH)
    grad_y = dot(coeffs * weight_y, cosine_full, HIGH)
    stacked = jnp.stack([grad_x, grad_y], axis=0)
    back = lax.all_to_all(stacked, "row", split_axis=2, concat_axis=1, tiled=True)
    pieces = lax.all_gather(back, "col", axis=1, tiled=True)
    cosine_cols = lax.dynamic_slice_in_dim(cosine_full, start, tile_cols, axis=1)
    sine_cols = lax.dynamic_slice_in_dim(sine_full, start, tile_cols, axis=1)
    field_x = dot_t(pieces[0], cosine_cols, HIGH)
    field_y = dot_t(pieces[1], sine_cols, HIGH)
    fields = jnp.stack([field_x.reshape(-1), field_y.reshape(-1)], axis=0)
    push = -areas[None, :] * gather_rows(fields, bin_ids, HIGH)
    slot_count = margin_bin.shape[2]
    blocks = n_rows * n_cols
    outgoing = push.reshape(2, blocks, slot_count).transpose(1, 0, 2).reshape(blocks, 2 * slot_count)
    incoming = lax.all_to_all(outgoing, ("row", "col"), split_axis=0, concat_axis=0, tiled=True)
    incoming = incoming.reshape(blocks, 2, slot_count).transpose(1, 0, 2).reshape(2, blocks * slot_count)
    owners = margin_cell[0].reshape(-1)
    wire_grad = scatter_rows(pin_grad, pin_cell[0], positions.shape[1], HIGH)
    return wire_grad + scatter_rows(incoming, owners, positions.shape[1], HIGH)


def solution(mesh):
    placed = (
        P(None, ("row", "col")),
        P(None, ("row", "col"), None),
        P(("row", "col"), None),
        P(("row", "col"), None),
        P(("row", "col"), None),
        P(("row", "col"), None, None),
        P(("row", "col"), None, None),
        P(("row", "col"), None, None),
    )
    return jax.shard_map(
        local, mesh=mesh, in_specs=placed, out_specs=P(None, ("row", "col")), check_vma=False
    )
```

```python
import jax
import jax.numpy as jnp
from jax import lax
from jax.sharding import PartitionSpec as P

NB = 2048


GAMMA_BINS = 8.0
HIGH = lax.Precision.HIGH
HIGHEST = lax.Precision.HIGHEST
STEPS = (1, 2, 4, 8, 16)


def trig_tables(frequency, position, length):
    residue = frequency * (2 * position + 1) % (4 * length)
    angles = residue.astype(jnp.float32) * (jnp.pi / (2.0 * length))
    return (jnp.cos(angles), jnp.sin(angles))


def full_tables(length):
    odd = 2 * lax.optimization_barrier(jnp.arange(length, dtype=jnp.int32)) + 1
    upper = (jnp.arange(length // 32, dtype=jnp.int32) * 32)[:, None] * odd[None, :] % (4 * length)
    lower = jnp.arange(32, dtype=jnp.int32)[:, None] * odd[None, :] % (4 * length)
    step = jnp.pi / (2.0 * length)
    cos_a, sin_a = jnp.cos(upper.astype(jnp.float32) * step), jnp.sin(upper.astype(jnp.float32) * step)
    cos_b, sin_b = jnp.cos(lower.astype(jnp.float32) * step), jnp.sin(lower.astype(jnp.float32) * step)
    cosine = cos_a[:, None, :] * cos_b[None, :, :] - sin_a[:, None, :] * sin_b[None, :, :]
    sine = sin_a[:, None, :] * cos_b[None, :, :] + cos_a[:, None, :] * sin_b[None, :, :]
    return cosine.reshape(length, length), sine.reshape(length, length)


def spectral_scale(frequency):
    return jnp.where(frequency == 0, 1.0, 2.0).astype(jnp.float32) / NB


def field_weights(freq_u, freq_v):
    omega_u = freq_u.astype(jnp.float32) * (jnp.pi / NB)
    omega_v = freq_v.astype(jnp.float32) * (jnp.pi / NB)
    anchor = ((freq_u == 0) & (freq_v == 0)).astype(jnp.float32)
    denominator = omega_u * omega_u + omega_v * omega_v + anchor
    return (omega_u / denominator, omega_v / denominator)


def dot(left, right, precision):
    return jnp.dot(left, right, precision=precision, preferred_element_type=jnp.float32)


def dot_t(left, right, precision):
    return lax.dot_general(
        left, right, (((0,), (0,)), ((), ())), precision=precision,
        preferred_element_type=jnp.float32,
    )


def one_hot(ids, count):
    return (ids[:, None] == jnp.arange(count, dtype=ids.dtype)[None, :]).astype(jnp.float32)


def gather_rows(values, ids, precision):
    channels, size = values.shape
    table = values.reshape(channels, size // 128, 128).transpose(1, 0, 2).reshape(size // 128, channels * 128)
    picked = lax.dot_general(
        table, one_hot(ids // 128, size // 128), (((0,), (1,)), ((), ())), precision=precision,
        preferred_element_type=jnp.float32,
    ).reshape(channels, 128, ids.shape[0])
    lane = jnp.arange(128, dtype=ids.dtype)[:, None] == (ids % 128)[None, :]
    return jnp.sum(jnp.where(lane[None], picked, 0.0), axis=1)


def scatter_rows(values, ids, size, precision):
    channels, count = values.shape
    lane = (jnp.arange(128, dtype=ids.dtype)[:, None] == (ids % 128)[None, :]).astype(jnp.float32)
    spread = (values[:, None, :] * lane[None, :, :]).reshape(channels * 128, count)
    summed = dot(spread, one_hot(ids // 128, size // 128), precision)
    return summed.reshape(channels, 128, size // 128).transpose(0, 2, 1).reshape(channels, size)


def shift_prev(x, s, fill):
    pad = jnp.full(x.shape[:-1] + (s,), fill, x.dtype)
    return jnp.concatenate([pad, x[..., :-s]], axis=-1)


def shift_next(x, s, fill):
    pad = jnp.full(x.shape[:-1] + (s,), fill, x.dtype)
    return jnp.concatenate([x[..., s:], pad], axis=-1)


def wirelength(cell_pos, offsets, weights, cell_ids, net_ids):
    pin_pos = gather_rows(cell_pos, cell_ids, HIGHEST) + offsets
    signed = jnp.concatenate([pin_pos, -pin_pos], axis=0)
    scores = signed / GAMMA_BINS
    prev_same = [shift_prev(net_ids, s, -1) == net_ids for s in STEPS]
    next_same = [shift_next(net_ids, s, -1) == net_ids for s in STEPS]
    maxima = scores
    for s, same in zip(STEPS, prev_same):
        maxima = jnp.where(same, jnp.maximum(maxima, shift_prev(maxima, s, 0.0)), maxima)
    for s, same in zip(STEPS, next_same):
        maxima = jnp.where(same, jnp.maximum(maxima, shift_next(maxima, s, 0.0)), maxima)
    exp_terms = jnp.exp(scores - maxima)
    sums = jnp.concatenate([exp_terms, signed * exp_terms], axis=0)
    for s, same in zip(STEPS, prev_same):
        sums = sums + jnp.where(same, shift_prev(sums, s, 0.0), 0.0)
    for s, same in zip(STEPS, next_same):
        sums = jnp.where(same, shift_next(sums, s, 0.0), sums)
    totals = sums[:4]
    centres = sums[4:] / totals
    slopes = exp_terms / totals * (1.0 + (signed - centres) / GAMMA_BINS)
    pin_weight = gather_rows(weights[None, :], net_ids, HIGHEST)[0]
    return (slopes[:2] - slopes[2:]) * pin_weight


def local(
    positions, pin_offset, net_weight, pin_cell, pin_net, margin_bin, margin_area, margin_cell
):
    n_rows = lax.axis_size("row")
    n_cols = lax.axis_size("col")
    tile_rows = NB // n_rows
    tile_cols = NB // n_cols
    row_index = lax.axis_index("row")
    col_index = lax.axis_index("col")
    bin_ids = margin_bin[0].reshape(-1)
    areas = margin_area[0].reshape(-1)
    tile_size = tile_rows * tile_cols
    density = scatter_rows(areas[None, :], bin_ids, tile_size, HIGH).reshape(tile_rows, tile_cols)
    cosine_full, sine_full = full_tables(NB)
    start = col_index * tile_cols
    part_in = lax.all_gather(density, "col", axis=1, tiled=True)
    cosine_rows = lax.dynamic_slice_in_dim(cosine_full, start, tile_cols, axis=0)
    cols_mine = start + jnp.arange(tile_cols, dtype=jnp.int32)
    spectral = lax.dot_general(
        cosine_rows, part_in, (((1,), (1,)), ((), ())), precision=HIGH,
        preferred_element_type=jnp.float32,
    ) * spectral_scale(cols_mine)[:, None]
    strip = lax.all_to_all(spectral, "row", split_axis=0, concat_axis=1, tiled=True)
    width = tile_cols // n_rows
    v_mine = start + row_index * width + jnp.arange(width, dtype=jnp.int32)
    frequency = jnp.arange(NB, dtype=jnp.int32)
    coeffs = lax.dot_general(
        strip, cosine_full, (((1,), (1,)), ((), ())), precision=HIGH,
        preferred_element_type=jnp.float32,
    ) * spectral_scale(frequency)[None, :]
    weight_x, weight_y = field_weights(frequency[None, :], v_mine[:, None])
    grad_x = dot(coeffs * weight_x, sine_full, HIGH)
    grad_y = dot(coeffs * weight_y, cosine_full, HIGH)
    stacked = jnp.stack([grad_x, grad_y], axis=0)
    back = lax.all_to_all(stacked, "row", split_axis=2, concat_axis=1, tiled=True)
    wire_inputs, back = lax.optimization_barrier(
        ((positions, pin_offset[:, 0, :], net_weight[0], pin_cell[0], pin_net[0]), back)
    )
    pin_grad = wirelength(*wire_inputs)
    pieces = lax.all_gather(back, "col", axis=1, tiled=True)
    cosine_cols = lax.dynamic_slice_in_dim(cosine_full, start, tile_cols, axis=1)
    sine_cols = lax.dynamic_slice_in_dim(sine_full, start, tile_cols, axis=1)
    field_x = dot_t(pieces[0], cosine_cols, HIGH)
    field_y = dot_t(pieces[1], sine_cols, HIGH)
    fields = jnp.stack([field_x.reshape(-1), field_y.reshape(-1)], axis=0)
    push = -areas[None, :] * gather_rows(fields, bin_ids, HIGH)
    slot_count = margin_bin.shape[2]
    blocks = n_rows * n_cols
    outgoing = push.reshape(2, blocks, slot_count).transpose(1, 0, 2).reshape(blocks, 2 * slot_count)
    incoming = lax.all_to_all(outgoing, ("row", "col"), split_axis=0, concat_axis=0, tiled=True)
    incoming = incoming.reshape(blocks, 2, slot_count).transpose(1, 0, 2).reshape(2, blocks * slot_count)
    owners = margin_cell[0].reshape(-1)
    wire_grad = scatter_rows(pin_grad, pin_cell[0], positions.shape[1], HIGH)
    return wire_grad + scatter_rows(incoming, owners, positions.shape[1], HIGH)


def solution(mesh):
    placed = (
        P(None, ("row", "col")),
        P(None, ("row", "col"), None),
        P(("row", "col"), None),
        P(("row", "col"), None),
        P(("row", "col"), None),
        P(("row", "col"), None, None),
        P(("row", "col"), None, None),
        P(("row", "col"), None, None),
    )
    return jax.shard_map(
        local, mesh=mesh, in_specs=placed, out_specs=P(None, ("row", "col")), check_vma=False
    )
```

```python
import jax
import jax.numpy as jnp
from jax import lax
from jax.sharding import PartitionSpec as P

NB = 2048


GAMMA_BINS = 8.0
HIGH = lax.Precision.HIGH
HIGHEST = lax.Precision.HIGHEST
STEPS = (1, 2, 4, 8, 16)


def trig_tables(frequency, position, length):
    residue = frequency * (2 * position + 1) % (4 * length)
    angles = residue.astype(jnp.float32) * (jnp.pi / (2.0 * length))
    return (jnp.cos(angles), jnp.sin(angles))


def angle_tables(upper_u, lower_u, positions, length):
    odd = 2 * positions + 1
    step = jnp.pi / (2.0 * length)
    upper = (upper_u[:, None] * odd[None, :] % (4 * length)).astype(jnp.float32) * step
    lower = (lower_u[:, None] * odd[None, :] % (4 * length)).astype(jnp.float32) * step
    cos_a, sin_a = jnp.cos(upper)[:, None, :], jnp.sin(upper)[:, None, :]
    cos_b, sin_b = jnp.cos(lower)[None, :, :], jnp.sin(lower)[None, :, :]
    rows = upper_u.shape[0] * lower_u.shape[0]
    cosine = (cos_a * cos_b - sin_a * sin_b).reshape(rows, positions.shape[0])
    sine = (sin_a * cos_b + cos_a * sin_b).reshape(rows, positions.shape[0])
    return cosine, sine


def parity_tables(length, parity):
    half = length // 2
    positions = lax.optimization_barrier(jnp.arange(half, dtype=jnp.int32))
    upper_u = 64 * jnp.arange(half // 32, dtype=jnp.int32)
    lower_u = 2 * jnp.arange(32, dtype=jnp.int32) + parity
    return angle_tables(upper_u, lower_u, positions, length)


def block_tables(first, count, positions, length):
    upper_u = first + 32 * jnp.arange(count // 32, dtype=jnp.int32)
    return angle_tables(upper_u, jnp.arange(32, dtype=jnp.int32), positions, length)


def flip(x):
    return lax.rev(x, (x.ndim - 1,))


def spectral_scale(frequency):
    return jnp.where(frequency == 0, 1.0, 2.0).astype(jnp.float32) / NB


def field_weights(freq_u, freq_v):
    omega_u = freq_u.astype(jnp.float32) * (jnp.pi / NB)
    omega_v = freq_v.astype(jnp.float32) * (jnp.pi / NB)
    anchor = ((freq_u == 0) & (freq_v == 0)).astype(jnp.float32)
    denominator = omega_u * omega_u + omega_v * omega_v + anchor
    return (omega_u / denominator, omega_v / denominator)


def dot(left, right, precision):
    return jnp.dot(left, right, precision=precision, preferred_element_type=jnp.float32)


def dot_t(left, right, precision):
    return lax.dot_general(
        left, right, (((0,), (0,)), ((), ())), precision=precision,
        preferred_element_type=jnp.float32,
    )


def one_hot(ids, count):
    return (ids[:, None] == jnp.arange(count, dtype=ids.dtype)[None, :]).astype(jnp.float32)


def gather_rows(values, ids, precision):
    channels, size = values.shape
    table = values.reshape(channels, size // 128, 128).transpose(1, 0, 2).reshape(size // 128, channels * 128)
    picked = lax.dot_general(
        table, one_hot(ids // 128, size // 128), (((0,), (1,)), ((), ())), precision=precision,
        preferred_element_type=jnp.float32,
    ).reshape(channels, 128, ids.shape[0])
    lane = jnp.arange(128, dtype=ids.dtype)[:, None] == (ids % 128)[None, :]
    return jnp.sum(jnp.where(lane[None], picked, 0.0), axis=1)


def scatter_rows(values, ids, size, precision):
    channels, count = values.shape
    lane = (jnp.arange(128, dtype=ids.dtype)[:, None] == (ids % 128)[None, :]).astype(jnp.float32)
    spread = (values[:, None, :] * lane[None, :, :]).reshape(channels * 128, count)
    summed = dot(spread, one_hot(ids // 128, size // 128), precision)
    return summed.reshape(channels, 128, size // 128).transpose(0, 2, 1).reshape(channels, size)


def shift_prev(x, s, fill):
    pad = jnp.full(x.shape[:-1] + (s,), fill, x.dtype)
    return jnp.concatenate([pad, x[..., :-s]], axis=-1)


def shift_next(x, s, fill):
    pad = jnp.full(x.shape[:-1] + (s,), fill, x.dtype)
    return jnp.concatenate([x[..., s:], pad], axis=-1)


def wirelength(cell_pos, offsets, weights, cell_ids, net_ids):
    pin_pos = gather_rows(cell_pos, cell_ids, HIGHEST) + offsets
    signed = jnp.concatenate([pin_pos, -pin_pos], axis=0)
    scores = signed / GAMMA_BINS
    prev_same = [shift_prev(net_ids, s, -1) == net_ids for s in STEPS]
    next_same = [shift_next(net_ids, s, -1) == net_ids for s in STEPS]
    maxima = scores
    for s, same in zip(STEPS, prev_same):
        maxima = jnp.where(same, jnp.maximum(maxima, shift_prev(maxima, s, 0.0)), maxima)
    for s, same in zip(STEPS, next_same):
        maxima = jnp.where(same, jnp.maximum(maxima, shift_next(maxima, s, 0.0)), maxima)
    exp_terms = jnp.exp(scores - maxima)
    sums = jnp.concatenate([exp_terms, signed * exp_terms], axis=0)
    for s, same in zip(STEPS, prev_same):
        sums = sums + jnp.where(same, shift_prev(sums, s, 0.0), 0.0)
    for s, same in zip(STEPS, next_same):
        sums = jnp.where(same, shift_next(sums, s, 0.0), sums)
    totals = sums[:4]
    centres = sums[4:] / totals
    slopes = exp_terms / totals * (1.0 + (signed - centres) / GAMMA_BINS)
    pin_weight = gather_rows(weights[None, :], net_ids, HIGHEST)[0]
    return (slopes[:2] - slopes[2:]) * pin_weight


def local(
    positions, pin_offset, net_weight, pin_cell, pin_net, margin_bin, margin_area, margin_cell
):
    pin_grad = wirelength(positions, pin_offset[:, 0, :], net_weight[0], pin_cell[0], pin_net[0])
    n_rows = lax.axis_size("row")
    n_cols = lax.axis_size("col")
    tile_rows = NB // n_rows
    tile_cols = NB // n_cols
    row_index = lax.axis_index("row")
    col_index = lax.axis_index("col")
    bin_ids = margin_bin[0].reshape(-1)
    areas = margin_area[0].reshape(-1)
    tile_size = tile_rows * tile_cols
    density = scatter_rows(areas[None, :], bin_ids, tile_size, HIGH).reshape(tile_rows, tile_cols)
    start = col_index * tile_cols
    part_in = lax.all_gather(density, "col", axis=1, tiled=True)
    everywhere = jnp.arange(NB, dtype=jnp.int32)
    cols_mine = start + jnp.arange(tile_cols, dtype=jnp.int32)
    cosine_rows, _ = block_tables(start, tile_cols, everywhere, NB)
    spectral = lax.dot_general(
        cosine_rows, part_in, (((1,), (1,)), ((), ())), precision=HIGH,
        preferred_element_type=jnp.float32,
    ) * spectral_scale(cols_mine)[:, None]
    strip = lax.all_to_all(spectral, "row", split_axis=0, concat_axis=1, tiled=True)
    width = tile_cols // n_rows
    v_mine = start + row_index * width + jnp.arange(width, dtype=jnp.int32)
    half = NB // 2
    cos_even, sin_even = parity_tables(NB, 0)
    cos_odd, sin_odd = parity_tables(NB, 1)
    head, tail = strip[:, :half], flip(strip[:, half:])
    grads_x, grads_y = [], []
    for parity, table, x_part in ((0, cos_even, head + tail), (1, cos_odd, head - tail)):
        u_part = 2 * jnp.arange(half, dtype=jnp.int32) + parity
        coeffs = lax.dot_general(
            x_part, table, (((1,), (1,)), ((), ())), precision=HIGH,
            preferred_element_type=jnp.float32,
        ) * spectral_scale(u_part)[None, :]
        weight_x, weight_y = field_weights(u_part[None, :], v_mine[:, None])
        grads_x.append(dot(coeffs * weight_x, (sin_even, sin_odd)[parity], HIGH))
        grads_y.append(dot(coeffs * weight_y, (cos_even, cos_odd)[parity], HIGH))
    grad_x = jnp.concatenate([grads_x[0] + grads_x[1], flip(grads_x[1] - grads_x[0])], axis=1)
    grad_y = jnp.concatenate([grads_y[0] + grads_y[1], flip(grads_y[0] - grads_y[1])], axis=1)
    stacked = jnp.stack([grad_x, grad_y], axis=0)
    back = lax.all_to_all(stacked, "row", split_axis=2, concat_axis=1, tiled=True)
    pieces = lax.all_gather(back, "col", axis=1, tiled=True)
    cosine_cols, sine_cols = block_tables(0, NB, cols_mine, NB)
    field_x = dot_t(pieces[0], cosine_cols, HIGH)
    field_y = dot_t(pieces[1], sine_cols, HIGH)
    fields = jnp.stack([field_x.reshape(-1), field_y.reshape(-1)], axis=0)
    push = -areas[None, :] * gather_rows(fields, bin_ids, HIGH)
    slot_count = margin_bin.shape[2]
    blocks = n_rows * n_cols
    outgoing = push.reshape(2, blocks, slot_count).transpose(1, 0, 2).reshape(blocks, 2 * slot_count)
    incoming = lax.all_to_all(outgoing, ("row", "col"), split_axis=0, concat_axis=0, tiled=True)
    incoming = incoming.reshape(blocks, 2, slot_count).transpose(1, 0, 2).reshape(2, blocks * slot_count)
    owners = margin_cell[0].reshape(-1)
    wire_grad = scatter_rows(pin_grad, pin_cell[0], positions.shape[1], HIGH)
    return wire_grad + scatter_rows(incoming, owners, positions.shape[1], HIGH)


def solution(mesh):
    placed = (
        P(None, ("row", "col")),
        P(None, ("row", "col"), None),
        P(("row", "col"), None),
        P(("row", "col"), None),
        P(("row", "col"), None),
        P(("row", "col"), None, None),
        P(("row", "col"), None, None),
        P(("row", "col"), None, None),
    )
    return jax.shard_map(
        local, mesh=mesh, in_specs=placed, out_specs=P(None, ("row", "col")), check_vma=False
    )
```

```python
import jax
import jax.numpy as jnp
from jax import lax
from jax.sharding import PartitionSpec as P

NB = 2048


GAMMA_BINS = 8.0
HIGH = lax.Precision.HIGH
HIGHEST = lax.Precision.HIGHEST
STEPS = (1, 2, 4, 8, 16)


def trig_tables(frequency, position, length):
    residue = frequency * (2 * position + 1) % (4 * length)
    angles = residue.astype(jnp.float32) * (jnp.pi / (2.0 * length))
    return (jnp.cos(angles), jnp.sin(angles))


def angle_tables(upper_u, lower_u, positions, length):
    odd = 2 * positions + 1
    step = jnp.pi / (2.0 * length)
    upper = (upper_u[:, None] * odd[None, :] % (4 * length)).astype(jnp.float32) * step
    lower = (lower_u[:, None] * odd[None, :] % (4 * length)).astype(jnp.float32) * step
    cos_a, sin_a = jnp.cos(upper)[:, None, :], jnp.sin(upper)[:, None, :]
    cos_b, sin_b = jnp.cos(lower)[None, :, :], jnp.sin(lower)[None, :, :]
    rows = upper_u.shape[0] * lower_u.shape[0]
    cosine = (cos_a * cos_b - sin_a * sin_b).reshape(rows, positions.shape[0])
    sine = (sin_a * cos_b + cos_a * sin_b).reshape(rows, positions.shape[0])
    return cosine, sine


def parity_tables(length, parity):
    half = length // 2
    positions = lax.optimization_barrier(jnp.arange(half, dtype=jnp.int32))
    upper_u = 64 * jnp.arange(half // 32, dtype=jnp.int32)
    lower_u = 2 * jnp.arange(32, dtype=jnp.int32) + parity
    return angle_tables(upper_u, lower_u, positions, length)


def block_tables(first, count, positions, length):
    upper_u = first + 32 * jnp.arange(count // 32, dtype=jnp.int32)
    return angle_tables(upper_u, jnp.arange(32, dtype=jnp.int32), positions, length)


def flip(x):
    return lax.rev(x, (x.ndim - 1,))


def spectral_scale(frequency):
    return jnp.where(frequency == 0, 1.0, 2.0).astype(jnp.float32) / NB


def field_weights(freq_u, freq_v):
    omega_u = freq_u.astype(jnp.float32) * (jnp.pi / NB)
    omega_v = freq_v.astype(jnp.float32) * (jnp.pi / NB)
    anchor = ((freq_u == 0) & (freq_v == 0)).astype(jnp.float32)
    denominator = omega_u * omega_u + omega_v * omega_v + anchor
    return (omega_u / denominator, omega_v / denominator)


def dot(left, right, precision):
    return jnp.dot(left, right, precision=precision, preferred_element_type=jnp.float32)


def dot_t(left, right, precision):
    return lax.dot_general(
        left, right, (((0,), (0,)), ((), ())), precision=precision,
        preferred_element_type=jnp.float32,
    )


def one_hot(ids, count):
    return (ids[:, None] == jnp.arange(count, dtype=ids.dtype)[None, :]).astype(jnp.float32)


def gather_rows(values, ids, precision):
    channels, size = values.shape
    table = values.reshape(channels, size // 128, 128).transpose(1, 0, 2).reshape(size // 128, channels * 128)
    picked = lax.dot_general(
        table, one_hot(ids // 128, size // 128), (((0,), (1,)), ((), ())), precision=precision,
        preferred_element_type=jnp.float32,
    ).reshape(channels, 128, ids.shape[0])
    lane = jnp.arange(128, dtype=ids.dtype)[:, None] == (ids % 128)[None, :]
    return jnp.sum(jnp.where(lane[None], picked, 0.0), axis=1)


def scatter_rows(values, ids, size, precision):
    channels, count = values.shape
    lane = (jnp.arange(128, dtype=ids.dtype)[:, None] == (ids % 128)[None, :]).astype(jnp.float32)
    spread = (values[:, None, :] * lane[None, :, :]).reshape(channels * 128, count)
    summed = dot(spread, one_hot(ids // 128, size // 128), precision)
    return summed.reshape(channels, 128, size // 128).transpose(0, 2, 1).reshape(channels, size)


def shift_prev(x, s, fill):
    pad = jnp.full(x.shape[:-1] + (s,), fill, x.dtype)
    return jnp.concatenate([pad, x[..., :-s]], axis=-1)


def shift_next(x, s, fill):
    pad = jnp.full(x.shape[:-1] + (s,), fill, x.dtype)
    return jnp.concatenate([x[..., s:], pad], axis=-1)


def wirelength(cell_pos, offsets, weights, cell_ids, net_ids):
    pin_pos = gather_rows(cell_pos, cell_ids, HIGHEST) + offsets
    signed = jnp.concatenate([pin_pos, -pin_pos], axis=0)
    scores = signed / GAMMA_BINS
    prev_same = [shift_prev(net_ids, s, -1) == net_ids for s in STEPS]
    next_same = [shift_next(net_ids, s, -1) == net_ids for s in STEPS]
    maxima = scores
    for s, same in zip(STEPS, prev_same):
        maxima = jnp.where(same, jnp.maximum(maxima, shift_prev(maxima, s, 0.0)), maxima)
    for s, same in zip(STEPS, next_same):
        maxima = jnp.where(same, jnp.maximum(maxima, shift_next(maxima, s, 0.0)), maxima)
    exp_terms = jnp.exp(scores - maxima)
    sums = jnp.concatenate([exp_terms, signed * exp_terms], axis=0)
    for s, same in zip(STEPS, prev_same):
        sums = sums + jnp.where(same, shift_prev(sums, s, 0.0), 0.0)
    for s, same in zip(STEPS, next_same):
        sums = jnp.where(same, shift_next(sums, s, 0.0), sums)
    totals = sums[:4]
    centres = sums[4:] / totals
    slopes = exp_terms / totals * (1.0 + (signed - centres) / GAMMA_BINS)
    pin_weight = gather_rows(weights[None, :], net_ids, HIGHEST)[0]
    return (slopes[:2] - slopes[2:]) * pin_weight


def local(
    positions, pin_offset, net_weight, pin_cell, pin_net, margin_bin, margin_area, margin_cell
):
    n_rows = lax.axis_size("row")
    n_cols = lax.axis_size("col")
    tile_rows = NB // n_rows
    tile_cols = NB // n_cols
    row_index = lax.axis_index("row")
    col_index = lax.axis_index("col")
    bin_ids = margin_bin[0].reshape(-1)
    areas = margin_area[0].reshape(-1)
    tile_size = tile_rows * tile_cols
    density = scatter_rows(areas[None, :], bin_ids, tile_size, HIGH).reshape(tile_rows, tile_cols)
    start = col_index * tile_cols
    part_in = lax.all_gather(density, "col", axis=1, tiled=True)
    everywhere = jnp.arange(NB, dtype=jnp.int32)
    cols_mine = start + jnp.arange(tile_cols, dtype=jnp.int32)
    cosine_rows, _ = block_tables(start, tile_cols, everywhere, NB)
    spectral = lax.dot_general(
        cosine_rows, part_in, (((1,), (1,)), ((), ())), precision=HIGH,
        preferred_element_type=jnp.float32,
    ) * spectral_scale(cols_mine)[:, None]
    strip = lax.all_to_all(spectral, "row", split_axis=0, concat_axis=1, tiled=True)
    width = tile_cols // n_rows
    v_mine = start + row_index * width + jnp.arange(width, dtype=jnp.int32)
    half = NB // 2
    cos_even, sin_even = parity_tables(NB, 0)
    cos_odd, sin_odd = parity_tables(NB, 1)
    head, tail = strip[:, :half], flip(strip[:, half:])
    grads_x, grads_y = [], []
    for parity, table, x_part in ((0, cos_even, head + tail), (1, cos_odd, head - tail)):
        u_part = 2 * jnp.arange(half, dtype=jnp.int32) + parity
        coeffs = lax.dot_general(
            x_part, table, (((1,), (1,)), ((), ())), precision=HIGH,
            preferred_element_type=jnp.float32,
        ) * spectral_scale(u_part)[None, :]
        weight_x, weight_y = field_weights(u_part[None, :], v_mine[:, None])
        grads_x.append(dot(coeffs * weight_x, (sin_even, sin_odd)[parity], HIGH))
        grads_y.append(dot(coeffs * weight_y, (cos_even, cos_odd)[parity], HIGH))
    grad_x = jnp.concatenate([grads_x[0] + grads_x[1], flip(grads_x[1] - grads_x[0])], axis=1)
    grad_y = jnp.concatenate([grads_y[0] + grads_y[1], flip(grads_y[0] - grads_y[1])], axis=1)
    stacked = jnp.stack([grad_x, grad_y], axis=0)
    back = lax.all_to_all(stacked, "row", split_axis=2, concat_axis=1, tiled=True)
    wire_inputs, back = lax.optimization_barrier(
        ((positions, pin_offset[:, 0, :], net_weight[0], pin_cell[0], pin_net[0]), back)
    )
    pin_grad = wirelength(*wire_inputs)
    pieces = lax.all_gather(back, "col", axis=1, tiled=True)
    cosine_cols, sine_cols = block_tables(0, NB, cols_mine, NB)
    field_x = dot_t(pieces[0], cosine_cols, HIGH)
    field_y = dot_t(pieces[1], sine_cols, HIGH)
    fields = jnp.stack([field_x.reshape(-1), field_y.reshape(-1)], axis=0)
    push = -areas[None, :] * gather_rows(fields, bin_ids, HIGH)
    slot_count = margin_bin.shape[2]
    blocks = n_rows * n_cols
    outgoing = push.reshape(2, blocks, slot_count).transpose(1, 0, 2).reshape(blocks, 2 * slot_count)
    incoming = lax.all_to_all(outgoing, ("row", "col"), split_axis=0, concat_axis=0, tiled=True)
    incoming = incoming.reshape(blocks, 2, slot_count).transpose(1, 0, 2).reshape(2, blocks * slot_count)
    owners = margin_cell[0].reshape(-1)
    wire_grad = scatter_rows(pin_grad, pin_cell[0], positions.shape[1], HIGH)
    return wire_grad + scatter_rows(incoming, owners, positions.shape[1], HIGH)


def solution(mesh):
    placed = (
        P(None, ("row", "col")),
        P(None, ("row", "col"), None),
        P(("row", "col"), None),
        P(("row", "col"), None),
        P(("row", "col"), None),
        P(("row", "col"), None, None),
        P(("row", "col"), None, None),
        P(("row", "col"), None, None),
    )
    return jax.shard_map(
        local, mesh=mesh, in_specs=placed, out_specs=P(None, ("row", "col")), check_vma=False
    )
```

```python
import jax
import jax.numpy as jnp
from jax import lax
from jax.sharding import PartitionSpec as P

NB = 2048


GAMMA_BINS = 8.0
HIGH = lax.Precision.HIGH
HIGHEST = lax.Precision.HIGHEST
STEPS = (1, 2, 4, 8, 16)


def trig_tables(frequency, position, length):
    residue = frequency * (2 * position + 1) % (4 * length)
    angles = residue.astype(jnp.float32) * (jnp.pi / (2.0 * length))
    return (jnp.cos(angles), jnp.sin(angles))


def angle_tables(upper_u, lower_u, positions, length):
    odd = 2 * positions + 1
    step = jnp.pi / (2.0 * length)
    upper = (upper_u[:, None] * odd[None, :] % (4 * length)).astype(jnp.float32) * step
    lower = (lower_u[:, None] * odd[None, :] % (4 * length)).astype(jnp.float32) * step
    cos_a, sin_a = jnp.cos(upper)[:, None, :], jnp.sin(upper)[:, None, :]
    cos_b, sin_b = jnp.cos(lower)[None, :, :], jnp.sin(lower)[None, :, :]
    rows = upper_u.shape[0] * lower_u.shape[0]
    cosine = (cos_a * cos_b - sin_a * sin_b).reshape(rows, positions.shape[0])
    sine = (sin_a * cos_b + cos_a * sin_b).reshape(rows, positions.shape[0])
    return cosine, sine


def parity_tables(length, parity):
    half = length // 2
    positions = lax.optimization_barrier(jnp.arange(half, dtype=jnp.int32))
    upper_u = 64 * jnp.arange(half // 32, dtype=jnp.int32)
    lower_u = 2 * jnp.arange(32, dtype=jnp.int32) + parity
    return angle_tables(upper_u, lower_u, positions, length)


def block_tables(first, count, positions, length):
    upper_u = first + 32 * jnp.arange(count // 32, dtype=jnp.int32)
    return angle_tables(upper_u, jnp.arange(32, dtype=jnp.int32), positions, length)


def flip(x):
    return lax.rev(x, (x.ndim - 1,))


def spectral_scale(frequency):
    return jnp.where(frequency == 0, 1.0, 2.0).astype(jnp.float32) / NB


def field_weights(freq_u, freq_v):
    omega_u = freq_u.astype(jnp.float32) * (jnp.pi / NB)
    omega_v = freq_v.astype(jnp.float32) * (jnp.pi / NB)
    anchor = ((freq_u == 0) & (freq_v == 0)).astype(jnp.float32)
    denominator = omega_u * omega_u + omega_v * omega_v + anchor
    return (omega_u / denominator, omega_v / denominator)


def dot(left, right, precision):
    return jnp.dot(left, right, precision=precision, preferred_element_type=jnp.float32)


def dot_t(left, right, precision):
    return lax.dot_general(
        left, right, (((0,), (0,)), ((), ())), precision=precision,
        preferred_element_type=jnp.float32,
    )


def one_hot(ids, count):
    return (ids[:, None] == jnp.arange(count, dtype=ids.dtype)[None, :]).astype(jnp.float32)


def gather_rows(values, ids, precision):
    channels, size = values.shape
    table = values.reshape(channels, size // 128, 128).transpose(1, 0, 2).reshape(size // 128, channels * 128)
    picked = lax.dot_general(
        table, one_hot(ids // 128, size // 128), (((0,), (1,)), ((), ())), precision=precision,
        preferred_element_type=jnp.float32,
    ).reshape(channels, 128, ids.shape[0])
    lane = jnp.arange(128, dtype=ids.dtype)[:, None] == (ids % 128)[None, :]
    return jnp.sum(jnp.where(lane[None], picked, 0.0), axis=1)


def scatter_rows(values, ids, size, precision):
    channels, count = values.shape
    lane = (jnp.arange(128, dtype=ids.dtype)[:, None] == (ids % 128)[None, :]).astype(jnp.float32)
    spread = (values[:, None, :] * lane[None, :, :]).reshape(channels * 128, count)
    summed = dot(spread, one_hot(ids // 128, size // 128), precision)
    return summed.reshape(channels, 128, size // 128).transpose(0, 2, 1).reshape(channels, size)


def shift_prev(x, s, fill):
    pad = jnp.full(x.shape[:-1] + (s,), fill, x.dtype)
    return jnp.concatenate([pad, x[..., :-s]], axis=-1)


def shift_next(x, s, fill):
    pad = jnp.full(x.shape[:-1] + (s,), fill, x.dtype)
    return jnp.concatenate([x[..., s:], pad], axis=-1)


def wirelength(cell_pos, offsets, weights, cell_ids, net_ids):
    pin_pos = gather_rows(cell_pos, cell_ids, HIGHEST) + offsets
    signed = jnp.concatenate([pin_pos, -pin_pos], axis=0)
    scores = signed / GAMMA_BINS
    prev_same = [shift_prev(net_ids, s, -1) == net_ids for s in STEPS]
    next_same = [shift_next(net_ids, s, -1) == net_ids for s in STEPS]
    maxima = scores
    for s, same in zip(STEPS, prev_same):
        maxima = jnp.where(same, jnp.maximum(maxima, shift_prev(maxima, s, 0.0)), maxima)
    for s, same in zip(STEPS, next_same):
        maxima = jnp.where(same, jnp.maximum(maxima, shift_next(maxima, s, 0.0)), maxima)
    exp_terms = jnp.exp(scores - maxima)
    sums = jnp.concatenate([exp_terms, signed * exp_terms], axis=0)
    for s, same in zip(STEPS, prev_same):
        sums = sums + jnp.where(same, shift_prev(sums, s, 0.0), 0.0)
    for s, same in zip(STEPS, next_same):
        sums = jnp.where(same, shift_next(sums, s, 0.0), sums)
    totals = sums[:4]
    centres = sums[4:] / totals
    slopes = exp_terms / totals * (1.0 + (signed - centres) / GAMMA_BINS)
    pin_weight = gather_rows(weights[None, :], net_ids, HIGHEST)[0]
    return (slopes[:2] - slopes[2:]) * pin_weight


def local(
    positions, pin_offset, net_weight, pin_cell, pin_net, margin_bin, margin_area, margin_cell
):
    n_rows = lax.axis_size("row")
    n_cols = lax.axis_size("col")
    tile_rows = NB // n_rows
    tile_cols = NB // n_cols
    row_index = lax.axis_index("row")
    col_index = lax.axis_index("col")
    bin_ids = margin_bin[0].reshape(-1)
    areas = margin_area[0].reshape(-1)
    tile_size = tile_rows * tile_cols
    density = scatter_rows(areas[None, :], bin_ids, tile_size, HIGH).reshape(tile_rows, tile_cols)
    start = col_index * tile_cols
    part_in = lax.all_gather(density, "col", axis=1, tiled=True)
    everywhere = jnp.arange(NB, dtype=jnp.int32)
    cols_mine = start + jnp.arange(tile_cols, dtype=jnp.int32)
    cosine_rows, _ = block_tables(start, tile_cols, everywhere, NB)
    spectral = lax.dot_general(
        cosine_rows, part_in, (((1,), (1,)), ((), ())), precision=HIGH,
        preferred_element_type=jnp.float32,
    ) * spectral_scale(cols_mine)[:, None]
    strip = lax.all_to_all(spectral, "row", split_axis=0, concat_axis=1, tiled=True)
    width = tile_cols // n_rows
    v_mine = start + row_index * width + jnp.arange(width, dtype=jnp.int32)
    half = NB // 2
    cos_even, sin_even = parity_tables(NB, 0)
    cos_odd, sin_odd = parity_tables(NB, 1)
    head, tail = strip[:, :half], flip(strip[:, half:])
    grads_x, grads_y = [], []
    for parity, table, x_part in ((0, cos_even, head + tail), (1, cos_odd, head - tail)):
        u_part = 2 * jnp.arange(half, dtype=jnp.int32) + parity
        coeffs = lax.dot_general(
            x_part, table, (((1,), (1,)), ((), ())), precision=HIGH,
            preferred_element_type=jnp.float32,
        ) * spectral_scale(u_part)[None, :]
        weight_x, weight_y = field_weights(u_part[None, :], v_mine[:, None])
        grads_x.append(dot(coeffs * weight_x, (sin_even, sin_odd)[parity], HIGH))
        grads_y.append(dot(coeffs * weight_y, (cos_even, cos_odd)[parity], HIGH))
    grad_x = jnp.concatenate([grads_x[0] + grads_x[1], flip(grads_x[1] - grads_x[0])], axis=1)
    grad_y = jnp.concatenate([grads_y[0] + grads_y[1], flip(grads_y[0] - grads_y[1])], axis=1)
    stacked = jnp.stack([grad_x, grad_y], axis=0)
    back = lax.all_to_all(stacked, "row", split_axis=2, concat_axis=1, tiled=True)
    wire_inputs, owners, back = lax.optimization_barrier(
        ((positions, pin_offset[:, 0, :], net_weight[0], pin_cell[0], pin_net[0]), margin_cell[0], back)
    )
    pin_grad = wirelength(*wire_inputs)
    pieces = lax.all_gather(back, "col", axis=1, tiled=True)
    cosine_cols, sine_cols = block_tables(0, NB, cols_mine, NB)
    field_x = dot_t(pieces[0], cosine_cols, HIGH)
    field_y = dot_t(pieces[1], sine_cols, HIGH)
    fields = jnp.stack([field_x.reshape(-1), field_y.reshape(-1)], axis=0)
    push = -areas[None, :] * gather_rows(fields, bin_ids, HIGH)
    slot_count = margin_bin.shape[2]
    blocks = n_rows * n_cols
    outgoing = push.reshape(2, blocks, slot_count).transpose(1, 0, 2).reshape(blocks, 2 * slot_count)
    incoming = lax.all_to_all(outgoing, ("row", "col"), split_axis=0, concat_axis=0, tiled=True)
    incoming = incoming.reshape(blocks, 2, slot_count).transpose(1, 0, 2).reshape(2, blocks * slot_count)
    wire_grad = scatter_rows(pin_grad, wire_inputs[3], positions.shape[1], HIGH)
    return wire_grad + scatter_rows(incoming, owners.reshape(-1), positions.shape[1], HIGH)


def solution(mesh):
    placed = (
        P(None, ("row", "col")),
        P(None, ("row", "col"), None),
        P(("row", "col"), None),
        P(("row", "col"), None),
        P(("row", "col"), None),
        P(("row", "col"), None, None),
        P(("row", "col"), None, None),
        P(("row", "col"), None, None),
    )
    return jax.shard_map(
        local, mesh=mesh, in_specs=placed, out_specs=P(None, ("row", "col")), check_vma=False
    )
```

```python
import jax
import jax.numpy as jnp
from jax import lax
from jax.sharding import PartitionSpec as P

NB = 2048


GAMMA_BINS = 8.0
HIGH = lax.Precision.HIGH
HIGHEST = lax.Precision.HIGHEST
STEPS = (1, 2, 4, 8, 16)


def trig_tables(frequency, position, length):
    residue = frequency * (2 * position + 1) % (4 * length)
    angles = residue.astype(jnp.float32) * (jnp.pi / (2.0 * length))
    return (jnp.cos(angles), jnp.sin(angles))


def angle_tables(upper_u, lower_u, positions, length):
    odd = 2 * positions + 1
    step = jnp.pi / (2.0 * length)
    upper = (upper_u[:, None] * odd[None, :] % (4 * length)).astype(jnp.float32) * step
    lower = (lower_u[:, None] * odd[None, :] % (4 * length)).astype(jnp.float32) * step
    cos_a, sin_a = jnp.cos(upper)[:, None, :], jnp.sin(upper)[:, None, :]
    cos_b, sin_b = jnp.cos(lower)[None, :, :], jnp.sin(lower)[None, :, :]
    rows = upper_u.shape[0] * lower_u.shape[0]
    cosine = (cos_a * cos_b - sin_a * sin_b).reshape(rows, positions.shape[0])
    sine = (sin_a * cos_b + cos_a * sin_b).reshape(rows, positions.shape[0])
    return cosine, sine


def parity_tables(length, parity):
    half = length // 2
    positions = lax.optimization_barrier(jnp.arange(half, dtype=jnp.int32))
    upper_u = 64 * jnp.arange(half // 32, dtype=jnp.int32)
    lower_u = 2 * jnp.arange(32, dtype=jnp.int32) + parity
    return angle_tables(upper_u, lower_u, positions, length)


def block_tables(first, count, positions, length):
    upper_u = first + 32 * jnp.arange(count // 32, dtype=jnp.int32)
    return angle_tables(upper_u, jnp.arange(32, dtype=jnp.int32), positions, length)


def flip(x):
    return lax.rev(x, (x.ndim - 1,))


def spectral_scale(frequency):
    return jnp.where(frequency == 0, 1.0, 2.0).astype(jnp.float32) / NB


def field_weights(freq_u, freq_v):
    omega_u = freq_u.astype(jnp.float32) * (jnp.pi / NB)
    omega_v = freq_v.astype(jnp.float32) * (jnp.pi / NB)
    anchor = ((freq_u == 0) & (freq_v == 0)).astype(jnp.float32)
    denominator = omega_u * omega_u + omega_v * omega_v + anchor
    return (omega_u / denominator, omega_v / denominator)


def dot(left, right, precision):
    return jnp.dot(left, right, precision=precision, preferred_element_type=jnp.float32)


def dot_t(left, right, precision):
    return lax.dot_general(
        left, right, (((0,), (0,)), ((), ())), precision=precision,
        preferred_element_type=jnp.float32,
    )


def one_hot(ids, count):
    return (ids[:, None] == jnp.arange(count, dtype=ids.dtype)[None, :]).astype(jnp.float32)


def gather_rows(values, ids, precision):
    channels, size = values.shape
    table = values.reshape(channels, size // 128, 128).transpose(1, 0, 2).reshape(size // 128, channels * 128)
    picked = lax.dot_general(
        table, one_hot(ids // 128, size // 128), (((0,), (1,)), ((), ())), precision=precision,
        preferred_element_type=jnp.float32,
    ).reshape(channels, 128, ids.shape[0])
    lane = jnp.arange(128, dtype=ids.dtype)[:, None] == (ids % 128)[None, :]
    return jnp.sum(jnp.where(lane[None], picked, 0.0), axis=1)


def scatter_rows(values, ids, size, precision):
    channels, count = values.shape
    lane = (jnp.arange(128, dtype=ids.dtype)[:, None] == (ids % 128)[None, :]).astype(jnp.float32)
    spread = (values[:, None, :] * lane[None, :, :]).reshape(channels * 128, count)
    summed = dot(spread, one_hot(ids // 128, size // 128), precision)
    return summed.reshape(channels, 128, size // 128).transpose(0, 2, 1).reshape(channels, size)


def shift_prev(x, s, fill):
    pad = jnp.full(x.shape[:-1] + (s,), fill, x.dtype)
    return jnp.concatenate([pad, x[..., :-s]], axis=-1)


def shift_next(x, s, fill):
    pad = jnp.full(x.shape[:-1] + (s,), fill, x.dtype)
    return jnp.concatenate([x[..., s:], pad], axis=-1)


def wirelength(cell_pos, offsets, weights, cell_ids, net_ids):
    pin_pos = gather_rows(cell_pos, cell_ids, HIGHEST) + offsets
    signed = jnp.concatenate([pin_pos, -pin_pos], axis=0)
    scores = signed / GAMMA_BINS
    prev_same = [shift_prev(net_ids, s, -1) == net_ids for s in STEPS]
    next_same = [shift_next(net_ids, s, -1) == net_ids for s in STEPS]
    maxima = scores
    for s, same in zip(STEPS, prev_same):
        maxima = jnp.where(same, jnp.maximum(maxima, shift_prev(maxima, s, 0.0)), maxima)
    for s, same in zip(STEPS, next_same):
        maxima = jnp.where(same, jnp.maximum(maxima, shift_next(maxima, s, 0.0)), maxima)
    exp_terms = jnp.exp(scores - maxima)
    sums = jnp.concatenate([exp_terms, signed * exp_terms], axis=0)
    for s, same in zip(STEPS, prev_same):
        sums = sums + jnp.where(same, shift_prev(sums, s, 0.0), 0.0)
    for s, same in zip(STEPS, next_same):
        sums = jnp.where(same, shift_next(sums, s, 0.0), sums)
    totals = sums[:4]
    centres = sums[4:] / totals
    slopes = exp_terms / totals * (1.0 + (signed - centres) / GAMMA_BINS)
    pin_weight = gather_rows(weights[None, :], net_ids, HIGHEST)[0]
    return (slopes[:2] - slopes[2:]) * pin_weight


def local(
    positions, pin_offset, net_weight, pin_cell, pin_net, margin_bin, margin_area, margin_cell
):
    n_rows = lax.axis_size("row")
    n_cols = lax.axis_size("col")
    tile_rows = NB // n_rows
    tile_cols = NB // n_cols
    row_index = lax.axis_index("row")
    col_index = lax.axis_index("col")
    bin_ids = margin_bin[0].reshape(-1)
    areas = margin_area[0].reshape(-1)
    tile_size = tile_rows * tile_cols
    density = scatter_rows(areas[None, :], bin_ids, tile_size, HIGH).reshape(tile_rows, tile_cols)
    start = col_index * tile_cols
    part_in = lax.all_gather(density, "col", axis=1, tiled=True)
    everywhere = jnp.arange(NB, dtype=jnp.int32)
    cols_mine = start + jnp.arange(tile_cols, dtype=jnp.int32)
    cosine_rows, _ = block_tables(start, tile_cols, everywhere, NB)
    spectral = lax.dot_general(
        cosine_rows, part_in, (((1,), (1,)), ((), ())), precision=HIGH,
        preferred_element_type=jnp.float32,
    ) * spectral_scale(cols_mine)[:, None]
    strip = lax.all_to_all(spectral, "row", split_axis=0, concat_axis=1, tiled=True)
    width = tile_cols // n_rows
    v_mine = start + row_index * width + jnp.arange(width, dtype=jnp.int32)
    half = NB // 2
    cos_even, sin_even = parity_tables(NB, 0)
    cos_odd, sin_odd = parity_tables(NB, 1)
    head, tail = strip[:, :half], flip(strip[:, half:])
    grads_x, grads_y = [], []
    for parity, table, x_part in ((0, cos_even, head + tail), (1, cos_odd, head - tail)):
        u_part = 2 * jnp.arange(half, dtype=jnp.int32) + parity
        coeffs = lax.dot_general(
            x_part, table, (((1,), (1,)), ((), ())), precision=HIGH,
            preferred_element_type=jnp.float32,
        ) * spectral_scale(u_part)[None, :]
        weight_x, weight_y = field_weights(u_part[None, :], v_mine[:, None])
        grads_x.append(dot(coeffs * weight_x, (sin_even, sin_odd)[parity], HIGH))
        grads_y.append(dot(coeffs * weight_y, (cos_even, cos_odd)[parity], HIGH))
    grad_x = jnp.concatenate([grads_x[0] + grads_x[1], flip(grads_x[1] - grads_x[0])], axis=1)
    grad_y = jnp.concatenate([grads_y[0] + grads_y[1], flip(grads_y[0] - grads_y[1])], axis=1)
    stacked = jnp.stack([grad_x, grad_y], axis=0).reshape(2, width, n_rows, tile_rows).transpose(2, 0, 1, 3)
    back = lax.all_to_all(stacked.reshape(n_rows, 2 * width * tile_rows), "row", 0, 0, tiled=True)
    back = back.reshape(n_rows, 2, width, tile_rows).transpose(1, 0, 2, 3).reshape(2, tile_cols, tile_rows)
    wire_inputs, owners, back = lax.optimization_barrier(
        ((positions, pin_offset[:, 0, :], net_weight[0], pin_cell[0], pin_net[0]), margin_cell[0], back)
    )
    pin_grad = wirelength(*wire_inputs)
    pieces = lax.all_gather(back, "col", axis=1, tiled=True)
    cosine_cols, sine_cols = block_tables(0, NB, cols_mine, NB)
    field_x = dot_t(pieces[0], cosine_cols, HIGH)
    field_y = dot_t(pieces[1], sine_cols, HIGH)
    fields = jnp.stack([field_x.reshape(-1), field_y.reshape(-1)], axis=0)
    push = -areas[None, :] * gather_rows(fields, bin_ids, HIGH)
    slot_count = margin_bin.shape[2]
    blocks = n_rows * n_cols
    outgoing = push.reshape(2, blocks, slot_count).transpose(1, 0, 2).reshape(blocks, 2 * slot_count)
    incoming = lax.all_to_all(outgoing, ("row", "col"), split_axis=0, concat_axis=0, tiled=True)
    incoming = incoming.reshape(blocks, 2, slot_count).transpose(1, 0, 2).reshape(2, blocks * slot_count)
    wire_grad = scatter_rows(pin_grad, wire_inputs[3], positions.shape[1], HIGH)
    return wire_grad + scatter_rows(incoming, owners.reshape(-1), positions.shape[1], HIGH)


def solution(mesh):
    placed = (
        P(None, ("row", "col")),
        P(None, ("row", "col"), None),
        P(("row", "col"), None),
        P(("row", "col"), None),
        P(("row", "col"), None),
        P(("row", "col"), None, None),
        P(("row", "col"), None, None),
        P(("row", "col"), None, None),
    )
    return jax.shard_map(
        local, mesh=mesh, in_specs=placed, out_specs=P(None, ("row", "col")), check_vma=False
    )
```
